256 devices in a mesh: ctx: 32 (over y_hi, z, core), uly: 8 (over x, y_lo).
Axes of the slice: x: 4, y: 4 (y_hi: 2, y_lo: 2; y = y_hi * 2 + y_lo), z: 8, core: 2. Of those that a mesh axis runs over, the one named last changes fastest.
Arguments:
- queries: bfloat16 [32768, 4096], P(('ctx', 'uly')), may hold values from -200 to 200, as said below
- keys: bfloat16 [32768, 1024], P(('ctx', 'uly')), may hold values from -6 to 6, as said below
- values: bfloat16 [32768, 1024], P(('ctx', 'uly')), may hold values from -6 to 6
Outputs:
- attended: bfloat16 [32768, 4096], P(('ctx', 'uly'))
The draws below stay inside these ranges and needn't reach their ends.
Inputs may be any that keep to these rules, and one draw needn't show every extreme that they name: `queries`: entries of order one, except that some query rows may be large. `keys`: entries of order one.
All inputs are finite; a program needn't handle non-finite values.
Results may differ from the reference program's by a relative error of at most 0.0055.
Values may be sent and summed in bfloat16 or wider, within the bound.
No kernel may reach another device: no remote copies, remote signals or barrier semaphores. Data moves between devices by JAX's collectives and lax.ppermute only.
A program may use at most 64 MiB of HBM per device.

```python
import jax
import jax.numpy as jnp
from jax import lax

HQ = 32
KEY_VALUE_HEADS = 8
HEAD_SIZE = 128
WINDOW_BLOCKS = 3
QUERY_PER_KEY = 4
BLOCK_TOKENS = 1024
SEQUENCE_TOKENS = 32768
N_CTX = 32


def common_keys(key):
    base_offset = jax.random.normal(jax.random.fold_in(key, 11), (SEQUENCE_TOKENS, KEY_VALUE_HEADS * HEAD_SIZE), jnp.float32)
    base_offset = jnp.clip(base_offset, -4.5, 4.5)
    return base_offset


def draw_keys(key, part):
    return common_keys(key).astype(jnp.bfloat16)


def draw_queries(key, part):
    drawn_output = jax.random.normal(jax.random.fold_in(key, 12), (SEQUENCE_TOKENS, HQ * HEAD_SIZE), jnp.float32)
    drawn_output = jnp.clip(drawn_output, -4.5, 4.5)
    return drawn_output.astype(jnp.bfloat16)


def shard_levels(own_key, shape, split, low, largest):
    def one(dim, shards_of):
        steps = jax.random.uniform(jax.random.fold_in(jax.random.fold_in(own_key, 6), dim), (shards_of,), jnp.float32, low / len(split), largest / len(split))
        return jnp.repeat(jnp.exp(steps), shape[dim] // shards_of).reshape((-1,) + (1,) * (len(shape) - dim - 1))

    factor_of = one(*split[0])
    for cut in split[1:]:
        factor_of = factor_of * one(*cut)
    return factor_of


def scatter_about(stream_key, extent, spread, most, cuts=(), held_as=jnp.bfloat16):
    result = jax.random.normal(stream_key, extent, jnp.float32) * spread
    if len(cuts) > 0:
        result = shard_levels(stream_key, extent, cuts, -0.22, 0.18) * result
    return jnp.clip(result, min=-most, max=most).astype(held_as)


def setup_inputs(seed: int = 0) -> dict:
    arg_keys = jax.random.split(jax.random.key(seed), 4)
    return {
        "queries": draw_queries(jax.random.fold_in(arg_keys[3], 71), 0),
        "keys": draw_keys(jax.random.fold_in(arg_keys[3], 71), 0),
        "values": scatter_about(arg_keys[2], (SEQUENCE_TOKENS, KEY_VALUE_HEADS * HEAD_SIZE), 1.0, 6.0, ((0, 256),)),
    }


def reference(queries, keys, values):
    scale_factor = HEAD_SIZE ** -0.5
    window = (WINDOW_BLOCKS + 1) * BLOCK_TOKENS
    front_block = jnp.zeros((WINDOW_BLOCKS * BLOCK_TOKENS, KEY_VALUE_HEADS * HEAD_SIZE), jnp.bfloat16)
    padded_keys = jnp.concatenate([front_block, keys], axis=0).reshape(SEQUENCE_TOKENS + WINDOW_BLOCKS * BLOCK_TOKENS, KEY_VALUE_HEADS, HEAD_SIZE)
    padded_values = jnp.concatenate([front_block, values], axis=0).reshape(SEQUENCE_TOKENS + WINDOW_BLOCKS * BLOCK_TOKENS, KEY_VALUE_HEADS, HEAD_SIZE)
    query_lattice = queries.reshape(SEQUENCE_TOKENS, KEY_VALUE_HEADS, QUERY_PER_KEY, HEAD_SIZE)

    def single_entry(index_value):
        block_number = index_value // KEY_VALUE_HEADS
        key_value_index = index_value % KEY_VALUE_HEADS
        start = (block_number * BLOCK_TOKENS).astype(jnp.int32)
        zero_index = jnp.int32(0)
        query_part = lax.dynamic_slice(query_lattice, (start, key_value_index, zero_index, zero_index), (BLOCK_TOKENS, 1, QUERY_PER_KEY, HEAD_SIZE))[:, 0].astype(jnp.float32)
        key_part = lax.dynamic_slice(padded_keys, (start, key_value_index, zero_index), (window, 1, HEAD_SIZE))[:, 0].astype(jnp.float32)
        value_part = lax.dynamic_slice(padded_values, (start, key_value_index, zero_index), (window, 1, HEAD_SIZE))[:, 0].astype(jnp.float32)
        scores = jnp.einsum("qgd,td->gqt", query_part, key_part) * scale_factor
        query_pos = start + jnp.arange(BLOCK_TOKENS, dtype=jnp.int32)
        key_pos = start - WINDOW_BLOCKS * BLOCK_TOKENS + jnp.arange(window, dtype=jnp.int32)
        visible = (key_pos[None, :] >= 0) & (key_pos[None, :] <= query_pos[:, None])
        scores = jnp.where(visible[None], scores, jnp.float32(-1e30))
        highest = jnp.max(scores, axis=-1, keepdims=True)
        weights = jnp.where(visible[None], jnp.exp(scores - highest), jnp.float32(0.0))
        totals = jnp.sum(weights, axis=-1)
        rounded = lax.optimization_barrier(weights.astype(jnp.bfloat16)).astype(jnp.float32)
        mixed = jnp.einsum("gqt,td->gqd", rounded, value_part) / totals[..., None]
        return mixed.astype(jnp.bfloat16)

    output_list = lax.map(single_entry, jnp.arange(N_CTX * KEY_VALUE_HEADS, dtype=jnp.int32))
    output_list = output_list.reshape(N_CTX, KEY_VALUE_HEADS, QUERY_PER_KEY, BLOCK_TOKENS, HEAD_SIZE).transpose(0, 3, 1, 2, 4)
    return output_list.reshape(SEQUENCE_TOKENS, HQ * HEAD_SIZE)
```

```python
import functools

import jax
import jax.numpy as jnp
from jax import lax
from jax.experimental import pallas as pl
from jax.experimental.pallas import tpu as pltpu
from jax.sharding import PartitionSpec as P

HEAD_SIZE = 128
WINDOW_BLOCKS = 3
TILE = 512


def passed_along(block, axis, distance):
    devices = range(lax.axis_size(axis))
    route = [(i - distance, i) for i in devices if i - distance in devices]
    return lax.ppermute(block, axis, route)


def attend_kernel(pos_ref, q_ref, k_ref, v_ref, o_ref, m_ref, l_ref, acc_ref, *, block_len):
    i = pl.program_id(1)
    cycle_pos = pos_ref[0]
    scale_factor = HEAD_SIZE ** (-0.5)
    q = q_ref[...]
    m_ref[...] = jnp.full(m_ref.shape, -jnp.inf, jnp.float32)
    l_ref[...] = jnp.zeros(l_ref.shape, jnp.float32)
    acc_ref[...] = jnp.zeros(acc_ref.shape, jnp.float32)

    def process(start, masked):
        k = k_ref[pl.ds(start, TILE), :]
        v = v_ref[pl.ds(start, TILE), :]
        s = lax.dot_general(q, k, (((1,), (1,)), ((), ())), preferred_element_type=jnp.float32)
        s = s * scale_factor
        if masked:
            rows = lax.broadcasted_iota(jnp.int32, s.shape, 0)
            cols = lax.broadcasted_iota(jnp.int32, s.shape, 1)
            s = jnp.where(cols <= rows, s, jnp.float32(-1e30))
        m_old = m_ref[...]
        m_new = jnp.maximum(m_old, jnp.max(s, axis=-1, keepdims=True))
        p = jnp.exp(s - m_new)
        factor = jnp.exp(m_old - m_new)
        l_ref[...] = l_ref[...] * factor + jnp.sum(p, axis=-1, keepdims=True)
        pv = jnp.dot(p.astype(jnp.bfloat16), v, preferred_element_type=jnp.float32)
        acc_ref[...] = acc_ref[...] * factor + pv
        m_ref[...] = m_new

    diag = WINDOW_BLOCKS * block_len
    process(pl.multiple_of(diag + i * TILE, TILE), True)
    tiles = block_len // TILE
    for t in range(tiles - 1):
        @pl.when(i > t)
        def _():
            process(diag + t * TILE, False)

    for back in range(1, WINDOW_BLOCKS + 1):
        base = (WINDOW_BLOCKS - back) * block_len

        @pl.when(cycle_pos >= back)
        def _():
            for t in range(tiles):
                process(base + t * TILE, False)

    o_ref[...] = (acc_ref[...] / l_ref[...]).astype(o_ref.dtype)


def attend(cycle_pos, query_here, key_all, value_all):
    block_len, width = query_here.shape
    q_heads = width // HEAD_SIZE
    window = key_all.shape[0]
    kernel = functools.partial(attend_kernel, block_len=block_len)
    grid_spec = pltpu.PrefetchScalarGridSpec(
        num_scalar_prefetch=1,
        grid=(q_heads, block_len // TILE),
        in_specs=[
            pl.BlockSpec((TILE, HEAD_SIZE), lambda h, i, pos: (i, h)),
            pl.BlockSpec((window, HEAD_SIZE), lambda h, i, pos: (0, 0)),
            pl.BlockSpec((window, HEAD_SIZE), lambda h, i, pos: (0, 0)),
        ],
        out_specs=pl.BlockSpec((TILE, HEAD_SIZE), lambda h, i, pos: (i, h)),
        scratch_shapes=[
            pltpu.VMEM((TILE, 1), jnp.float32),
            pltpu.VMEM((TILE, 1), jnp.float32),
            pltpu.VMEM((TILE, HEAD_SIZE), jnp.float32),
        ],
    )
    return pl.pallas_call(
        kernel,
        grid_spec=grid_spec,
        out_shape=jax.ShapeDtypeStruct((block_len, width), jnp.bfloat16),
        compiler_params=pltpu.CompilerParams(dimension_semantics=("arbitrary", "arbitrary")),
    )(cycle_pos, query_here, key_all, value_all)


def on_device(queries, keys, values):
    cycle_pos = lax.axis_index("ctx")
    query_here, key_here, value_here = (
        lax.all_to_all(queries, "uly", split_axis=1, concat_axis=0, tiled=True),
        lax.all_to_all(keys, "uly", split_axis=1, concat_axis=0, tiled=True),
        lax.all_to_all(values, "uly", split_axis=1, concat_axis=0, tiled=True),
    )
    key_list = [key_here]
    value_list = [value_here]
    current = (key_here, value_here)
    for step_back in range(1, WINDOW_BLOCKS + 1):
        current = passed_along((current[0], current[1]), "ctx", 1)
        key_list.insert(0, current[0])
        value_list.insert(0, current[1])
    key_all = jnp.concatenate(key_list, axis=0)
    value_all = jnp.concatenate(value_list, axis=0)
    pos = jnp.reshape(cycle_pos, (1,)).astype(jnp.int32)
    output_rows = attend(pos, query_here, key_all, value_all)
    return lax.all_to_all(output_rows, "uly", split_axis=0, concat_axis=1, tiled=True)


def solution(mesh):
    placed = (P(("ctx", "uly"), None), P(("ctx", "uly"), None), P(("ctx", "uly"), None))
    return jax.shard_map(
        on_device, mesh=mesh, in_specs=placed, out_specs=P(("ctx", "uly"), None), check_vma=False
    )
```

```python
import functools

import jax
import jax.numpy as jnp
from jax import lax
from jax.experimental import pallas as pl
from jax.experimental.pallas import tpu as pltpu
from jax.sharding import PartitionSpec as P

HEAD_SIZE = 128
WINDOW_BLOCKS = 3
KEY_TILE = 1024
LOG2_E = 1.4426950408889634


def passed_along(block, axis, distance):
    devices = range(lax.axis_size(axis))
    route = [(i - distance, i) for i in devices if i - distance in devices]
    return lax.ppermute(block, axis, route)


def attend_kernel(pos_ref, q_ref, kv0_ref, kv1_ref, kv2_ref, kv3_ref, o_ref, m_ref, l_ref, acc_ref, *, block_len):
    cycle_pos = pos_ref[0]
    exp_scale = HEAD_SIZE ** (-0.5) * LOG2_E
    q = q_ref[...]
    tile = min(KEY_TILE, block_len)
    m_ref[...] = jnp.full(m_ref.shape, -jnp.inf, jnp.float32)
    l_ref[...] = jnp.zeros(l_ref.shape, jnp.float32)
    acc_ref[...] = jnp.zeros(acc_ref.shape, jnp.float32)

    def process(kv_ref, start, masked):
        k = kv_ref[pl.ds(start, tile), pl.ds(0, HEAD_SIZE)]
        v = kv_ref[pl.ds(start, tile), pl.ds(HEAD_SIZE, HEAD_SIZE)]
        s = lax.dot_general(k, q, (((1,), (1,)), ((), ())), preferred_element_type=jnp.float32)
        if masked:
            keys = lax.broadcasted_iota(jnp.int32, s.shape, 0) + start
            rows = lax.broadcasted_iota(jnp.int32, s.shape, 1)
            s = jnp.where(keys <= rows, s, jnp.float32(-1e30))
        m_old = m_ref[...]
        m_new = jnp.maximum(m_old, jnp.max(s, axis=0, keepdims=True))
        p = jnp.exp2((s - m_new) * exp_scale)
        factor = jnp.exp2((m_old - m_new) * exp_scale)
        l_ref[...] = l_ref[...] * factor + jnp.sum(p, axis=0, keepdims=True)
        pv = lax.dot_general(
            v, p.astype(jnp.bfloat16), (((0,), (0,)), ((), ())), preferred_element_type=jnp.float32
        )
        acc_ref[...] = acc_ref[...] * factor + pv
        m_ref[...] = m_new

    for t in range(block_len // tile):
        process(kv3_ref, t * tile, True)
    for back, kv_ref in ((1, kv2_ref), (2, kv1_ref), (3, kv0_ref)):
        @pl.when(cycle_pos >= back)
        def _():
            for t in range(block_len // tile):
                process(kv_ref, t * tile, False)

    o_ref[...] = (acc_ref[...] / l_ref[...]).T.astype(o_ref.dtype)


def attend(pos, qkv, kv0, kv1, kv2, q_heads):
    block_len = qkv.shape[0]
    kernel = functools.partial(attend_kernel, block_len=block_len)
    kv_spec = pl.BlockSpec((block_len, 2 * HEAD_SIZE), lambda h, pos: (0, 0))
    grid_spec = pltpu.PrefetchScalarGridSpec(
        num_scalar_prefetch=1,
        grid=(q_heads,),
        in_specs=[
            pl.BlockSpec((block_len, HEAD_SIZE), lambda h, pos: (0, h)),
            kv_spec,
            kv_spec,
            kv_spec,
            pl.BlockSpec((block_len, 2 * HEAD_SIZE), lambda h, pos: (0, q_heads // 2)),
        ],
        out_specs=pl.BlockSpec((block_len, HEAD_SIZE), lambda h, pos: (0, h)),
        scratch_shapes=[
            pltpu.VMEM((1, block_len), jnp.float32),
            pltpu.VMEM((1, block_len), jnp.float32),
            pltpu.VMEM((HEAD_SIZE, block_len), jnp.float32),
        ],
    )
    return pl.pallas_call(
        kernel,
        grid_spec=grid_spec,
        out_shape=jax.ShapeDtypeStruct((block_len, q_heads * HEAD_SIZE), jnp.bfloat16),
        compiler_params=pltpu.CompilerParams(dimension_semantics=("arbitrary",)),
    )(pos, qkv, kv0, kv1, kv2, qkv)


def on_device(queries, keys, values):
    n = lax.axis_size("uly")
    rows = queries.shape[0]
    cycle_pos = lax.axis_index("ctx")
    packed = jnp.concatenate(
        [queries.reshape(rows, n, -1), keys.reshape(rows, n, -1), values.reshape(rows, n, -1)], axis=2
    )
    qkv = lax.all_to_all(packed, "uly", split_axis=1, concat_axis=0, tiled=True)
    qkv = qkv.reshape(rows * n, -1)
    q_heads = (qkv.shape[1] - 2 * HEAD_SIZE) // HEAD_SIZE
    kv_own = qkv[:, q_heads * HEAD_SIZE:]
    kv1 = passed_along(kv_own, "ctx", 1)
    kv2 = passed_along(kv1, "ctx", 1)
    kv3 = passed_along(kv2, "ctx", 1)
    pos = jnp.reshape(cycle_pos, (1,)).astype(jnp.int32)
    output_rows = attend(pos, qkv, kv3, kv2, kv1, q_heads)
    return lax.all_to_all(output_rows, "uly", split_axis=0, concat_axis=1, tiled=True)


def solution(mesh):
    placed = (P(("ctx", "uly"), None), P(("ctx", "uly"), None), P(("ctx", "uly"), None))
    return jax.shard_map(
        on_device, mesh=mesh, in_specs=placed, out_specs=P(("ctx", "uly"), None), check_vma=False
    )
```

```python
import functools

import jax
import jax.numpy as jnp
from jax import lax
from jax.experimental import pallas as pl
from jax.experimental.pallas import tpu as pltpu
from jax.sharding import PartitionSpec as P


HEAD_SIZE = 128
WINDOW_BLOCKS = 3
KEY_TILE = 1024
LOG2_E = 1.4426950408889634


def passed_along(block, axis, distance):
    devices = range(lax.axis_size(axis))
    route = [(i - distance, i) for i in devices if i - distance in devices]
    return lax.ppermute(block, axis, route)


def attend_kernel(pos_ref, q_ref, kv_ref, *refs, block_len, back, first, last):
    if first:
        o_refs, (m_ref, l_ref, acc_ref) = refs[:-3], refs[-3:]
    else:
        (m_in, l_in, acc_in), o_refs, (m_ref, l_ref, acc_ref) = refs[:3], refs[3:-3], refs[-3:]
    cycle_pos = pos_ref[0]
    exp_scale = HEAD_SIZE ** (-0.5) * LOG2_E
    tile = min(KEY_TILE, block_len)
    if first:
        m_ref[...] = jnp.full(m_ref.shape, -jnp.inf, jnp.float32)
        l_ref[...] = jnp.zeros(l_ref.shape, jnp.float32)
        acc_ref[...] = jnp.zeros(acc_ref.shape, jnp.float32)
    else:
        m_ref[...] = m_in[...]
        l_ref[...] = l_in[...]
        acc_ref[...] = acc_in[...]

    def process(start, masked):
        q = q_ref[...]
        k = kv_ref[pl.ds(start, tile), pl.ds(0, HEAD_SIZE)]
        v = kv_ref[pl.ds(start, tile), pl.ds(HEAD_SIZE, HEAD_SIZE)]
        s = lax.dot_general(k, q, (((1,), (1,)), ((), ())), preferred_element_type=jnp.float32)
        if masked:
            keys = lax.broadcasted_iota(jnp.int32, s.shape, 0) + start
            rows = lax.broadcasted_iota(jnp.int32, s.shape, 1)
            s = jnp.where(keys <= rows, s, jnp.float32(-1e30))
        m_old = m_ref[...]
        m_new = jnp.maximum(m_old, jnp.max(s, axis=0, keepdims=True))
        p = jnp.exp2((s - m_new) * exp_scale)
        factor = jnp.exp2((m_old - m_new) * exp_scale)
        l_ref[...] = l_ref[...] * factor + jnp.sum(p, axis=0, keepdims=True)
        pv = lax.dot_general(
            v, p.astype(jnp.bfloat16), (((0,), (0,)), ((), ())), preferred_element_type=jnp.float32
        )
        acc_ref[...] = acc_ref[...] * factor + pv
        m_ref[...] = m_new

    if back == 0:
        for t in range(block_len // tile):
            process(t * tile, True)
    else:
        @pl.when(cycle_pos >= back)
        def _():
            for t in range(block_len // tile):
                process(t * tile, False)

    if last:
        o_refs[0][...] = (acc_ref[...] / l_ref[...]).T.astype(o_refs[0].dtype)
    else:
        o_refs[0][...] = m_ref[...]
        o_refs[1][...] = l_ref[...]
        o_refs[2][...] = acc_ref[...]


def attend(pos, qkv, kv, carry, q_heads, back, kv_col):
    block_len = qkv.shape[0]
    first = carry is None
    last = back == WINDOW_BLOCKS
    kernel = functools.partial(attend_kernel, block_len=block_len, back=back, first=first, last=last)
    row_spec = pl.BlockSpec((None, 1, block_len), lambda h, pos: (h, 0, 0))
    acc_spec = pl.BlockSpec((None, HEAD_SIZE, block_len), lambda h, pos: (h, 0, 0))
    in_specs = [
        pl.BlockSpec((block_len, HEAD_SIZE), lambda h, pos: (0, h)),
        pl.BlockSpec((block_len, 2 * HEAD_SIZE), lambda h, pos: (0, kv_col)),
    ]
    operands = [pos, qkv, kv]
    if not first:
        in_specs += [row_spec, row_spec, acc_spec]
        operands += list(carry)
    carry_shapes = [
        jax.ShapeDtypeStruct((q_heads, 1, block_len), jnp.float32),
        jax.ShapeDtypeStruct((q_heads, 1, block_len), jnp.float32),
        jax.ShapeDtypeStruct((q_heads, HEAD_SIZE, block_len), jnp.float32),
    ]
    if last:
        out_specs = [pl.BlockSpec((block_len, HEAD_SIZE), lambda h, pos: (0, h))]
        out_shape = [jax.ShapeDtypeStruct((block_len, q_heads * HEAD_SIZE), jnp.bfloat16)]
        aliases = {}
    else:
        out_specs = [row_spec, row_spec, acc_spec]
        out_shape = carry_shapes
        aliases = {} if first else {3: 0, 4: 1, 5: 2}
    grid_spec = pltpu.PrefetchScalarGridSpec(
        num_scalar_prefetch=1,
        grid=(q_heads,),
        in_specs=in_specs,
        out_specs=out_specs,
        scratch_shapes=[
            pltpu.VMEM((1, block_len), jnp.float32),
            pltpu.VMEM((1, block_len), jnp.float32),
            pltpu.VMEM((HEAD_SIZE, block_len), jnp.float32),
        ],
    )
    result = pl.pallas_call(
        kernel,
        grid_spec=grid_spec,
        out_shape=out_shape,
        input_output_aliases=aliases,
        compiler_params=pltpu.CompilerParams(dimension_semantics=("arbitrary",)),
    )(*operands)
    return result[0] if last else tuple(result)


def on_device(queries, keys, values):
    n = lax.axis_size("uly")
    rows = queries.shape[0]
    cycle_pos = lax.axis_index("ctx")
    packed = jnp.concatenate(
        [queries.reshape(rows, n, -1), keys.reshape(rows, n, -1), values.reshape(rows, n, -1)], axis=2
    )
    qkv = lax.all_to_all(packed, "uly", split_axis=1, concat_axis=0, tiled=True)
    qkv = qkv.reshape(rows * n, -1)
    q_heads = (qkv.shape[1] - 2 * HEAD_SIZE) // HEAD_SIZE
    pos = jnp.reshape(cycle_pos, (1,)).astype(jnp.int32)
    kv = qkv[:, q_heads * HEAD_SIZE:]
    carry = attend(pos, qkv, qkv, None, q_heads, 0, q_heads // 2)
    for back in range(1, WINDOW_BLOCKS + 1):
        kv = passed_along(kv, "ctx", 1)
        carry = attend(pos, qkv, kv, carry, q_heads, back, 0)
    return lax.all_to_all(carry, "uly", split_axis=0, concat_axis=1, tiled=True)


def solution(mesh):
    placed = (P(("ctx", "uly"), None), P(("ctx", "uly"), None), P(("ctx", "uly"), None))
    return jax.shard_map(
        on_device, mesh=mesh, in_specs=placed, out_specs=P(("ctx", "uly"), None), check_vma=False
    )
```

```python
import functools

import jax
import jax.numpy as jnp
from jax import lax
from jax.experimental import pallas as pl
from jax.experimental.pallas import tpu as pltpu
from jax.sharding import PartitionSpec as P


HEAD_SIZE = 128
WINDOW_BLOCKS = 3
KEY_TILE = 1024
LOG2_E = 1.4426950408889634


def passed_along(block, axis, distance):
    devices = range(lax.axis_size(axis))
    route = [(i - distance, i) for i in devices if i - distance in devices]
    return lax.ppermute(block, axis, route)


def attend_kernel(pos_ref, q_ref, *refs, block_len, backs, first, last):
    n_kv = len(backs)
    kv_refs, refs = refs[:n_kv], refs[n_kv:]
    if first:
        o_refs, (m_ref, l_ref, acc_ref) = refs[:-3], refs[-3:]
    else:
        (m_in, l_in, acc_in), o_refs, (m_ref, l_ref, acc_ref) = refs[:3], refs[3:-3], refs[-3:]
    cycle_pos = pos_ref[0]
    exp_scale = HEAD_SIZE ** (-0.5) * LOG2_E
    tile = min(KEY_TILE, block_len)
    if first:
        m_ref[...] = jnp.full(m_ref.shape, -jnp.inf, jnp.float32)
        l_ref[...] = jnp.zeros(l_ref.shape, jnp.float32)
        acc_ref[...] = jnp.zeros(acc_ref.shape, jnp.float32)
    else:
        m_ref[...] = m_in[...]
        l_ref[...] = l_in[...]
        acc_ref[...] = acc_in[...]

    def process(kv_ref, start, masked):
        q = q_ref[...]
        k = kv_ref[pl.ds(start, tile), pl.ds(0, HEAD_SIZE)]
        v = kv_ref[pl.ds(start, tile), pl.ds(HEAD_SIZE, HEAD_SIZE)]
        s = lax.dot_general(k, q, (((1,), (1,)), ((), ())), preferred_element_type=jnp.float32)
        if masked:
            keys = lax.broadcasted_iota(jnp.int32, s.shape, 0) + start
            rows = lax.broadcasted_iota(jnp.int32, s.shape, 1)
            s = jnp.where(keys <= rows, s, jnp.float32(-1e30))
        m_old = m_ref[...]
        m_new = jnp.maximum(m_old, jnp.max(s, axis=0, keepdims=True))
        p = jnp.exp2((s - m_new) * exp_scale)
        factor = jnp.exp2((m_old - m_new) * exp_scale)
        l_ref[...] = l_ref[...] * factor + jnp.sum(p, axis=0, keepdims=True)
        pv = lax.dot_general(
            v, p.astype(jnp.bfloat16), (((0,), (0,)), ((), ())), preferred_element_type=jnp.float32
        )
        acc_ref[...] = acc_ref[...] * factor + pv
        m_ref[...] = m_new

    for back, kv_ref in zip(backs, kv_refs):
        if back == 0:
            for t in range(block_len // tile):
                process(kv_ref, t * tile, True)
        else:
            @pl.when(cycle_pos >= back)
            def _():
                for t in range(block_len // tile):
                    process(kv_ref, t * tile, False)

    if last:
        o_refs[0][...] = (acc_ref[...] / l_ref[...]).T.astype(o_refs[0].dtype)
    else:
        o_refs[0][...] = m_ref[...]
        o_refs[1][...] = l_ref[...]
        o_refs[2][...] = acc_ref[...]


def attend(pos, q_src, q_heads, kvs, carry, backs, last):
    block_len = q_src.shape[0]
    first = carry is None
    kernel = functools.partial(attend_kernel, block_len=block_len, backs=backs, first=first, last=last)
    row_spec = pl.BlockSpec((None, 1, block_len), lambda h, pos: (h, 0, 0))
    acc_spec = pl.BlockSpec((None, HEAD_SIZE, block_len), lambda h, pos: (h, 0, 0))
    in_specs = [pl.BlockSpec((block_len, HEAD_SIZE), lambda h, pos: (0, h))]
    operands = [pos, q_src]
    for kv, col in kvs:
        in_specs.append(pl.BlockSpec((block_len, 2 * HEAD_SIZE), lambda h, pos, col=col: (0, col)))
        operands.append(kv)
    if not first:
        in_specs += [row_spec, row_spec, acc_spec]
        operands += list(carry)
    if last:
        out_specs = [pl.BlockSpec((block_len, HEAD_SIZE), lambda h, pos: (0, h))]
        out_shape = [jax.ShapeDtypeStruct((block_len, q_heads * HEAD_SIZE), jnp.bfloat16)]
        aliases = {}
    else:
        out_specs = [row_spec, row_spec, acc_spec]
        out_shape = [
            jax.ShapeDtypeStruct((q_heads, 1, block_len), jnp.float32),
            jax.ShapeDtypeStruct((q_heads, 1, block_len), jnp.float32),
            jax.ShapeDtypeStruct((q_heads, HEAD_SIZE, block_len), jnp.float32),
        ]
        base = 2 + len(kvs)
        aliases = {} if first else {base: 0, base + 1: 1, base + 2: 2}
    grid_spec = pltpu.PrefetchScalarGridSpec(
        num_scalar_prefetch=1,
        grid=(q_heads,),
        in_specs=in_specs,
        out_specs=out_specs,
        scratch_shapes=[
            pltpu.VMEM((1, block_len), jnp.float32),
            pltpu.VMEM((1, block_len), jnp.float32),
            pltpu.VMEM((HEAD_SIZE, block_len), jnp.float32),
        ],
    )
    result = pl.pallas_call(
        kernel,
        grid_spec=grid_spec,
        out_shape=out_shape,
        input_output_aliases=aliases,
        compiler_params=pltpu.CompilerParams(dimension_semantics=("arbitrary",)),
    )(*operands)
    return result[0] if last else tuple(result)


def on_device(queries, keys, values):
    n = lax.axis_size("uly")
    rows = queries.shape[0]
    cycle_pos = lax.axis_index("ctx")
    pos = jnp.reshape(cycle_pos, (1,)).astype(jnp.int32)
    q_heads = queries.shape[1] // n // HEAD_SIZE
    half = q_heads // 2
    q_split = queries.reshape(rows, n, q_heads, HEAD_SIZE)
    packed = jnp.concatenate(
        [
            q_split[:, :, :half].reshape(rows, n, -1),
            keys.reshape(rows, n, -1),
            values.reshape(rows, n, -1),
        ],
        axis=2,
    )
    qkv = lax.all_to_all(packed, "uly", split_axis=1, concat_axis=0, tiled=True)
    qkv = qkv.reshape(rows * n, -1)
    q_rest = lax.all_to_all(
        q_split[:, :, half:].reshape(rows, n, -1), "uly", split_axis=1, concat_axis=0, tiled=True
    )
    q_rest = q_rest.reshape(rows * n, -1)
    kv_col = half // 2
    kv = qkv[:, half * HEAD_SIZE:]
    blocks = [(qkv, kv_col)]
    carry = attend(pos, qkv, half, [(qkv, kv_col)], None, (0,), False)
    for back in range(1, WINDOW_BLOCKS + 1):
        kv = passed_along(kv, "ctx", 1)
        blocks.append((kv, 0))
        carry = attend(pos, qkv, half, [(kv, 0)], carry, (back,), back == WINDOW_BLOCKS)
    out_front = lax.all_to_all(carry, "uly", split_axis=0, concat_axis=1, tiled=True)
    out_rest = attend(pos, q_rest, q_heads - half, blocks, None, tuple(range(WINDOW_BLOCKS + 1)), True)
    out_rest = lax.all_to_all(out_rest, "uly", split_axis=0, concat_axis=1, tiled=True)
    width = half * HEAD_SIZE
    return jnp.concatenate(
        [out_front.reshape(rows, n, width), out_rest.reshape(rows, n, width)], axis=2
    ).reshape(rows, -1)


def solution(mesh):
    placed = (P(("ctx", "uly"), None), P(("ctx", "uly"), None), P(("ctx", "uly"), None))
    return jax.shard_map(
        on_device, mesh=mesh, in_specs=placed, out_specs=P(("ctx", "uly"), None), check_vma=False
    )
```

```python
import functools

import jax
import jax.numpy as jnp
from jax import lax
from jax.experimental import pallas as pl
from jax.experimental.pallas import tpu as pltpu
from jax.sharding import PartitionSpec as P


HEAD_SIZE = 128
WINDOW_BLOCKS = 3
KEY_TILE = 1024
LOG2_E = 1.4426950408889634


def passed_along(block, axis, distance):
    devices = range(lax.axis_size(axis))
    route = [(i - distance, i) for i in devices if i - distance in devices]
    return lax.ppermute(block, axis, route)


def attend_kernel(pos_ref, q_ref, kv_ref, *refs, block_len, back, first, last):
    if first:
        o_refs, (m_ref, l_ref, acc_ref) = refs[:-3], refs[-3:]
    else:
        (m_in, l_in, acc_in), o_refs, (m_ref, l_ref, acc_ref) = refs[:3], refs[3:-3], refs[-3:]
    cycle_pos = pos_ref[0]
    exp_scale = HEAD_SIZE ** (-0.5) * LOG2_E
    tile = min(KEY_TILE, block_len)
    if first:
        m_ref[...] = jnp.full(m_ref.shape, -jnp.inf, jnp.float32)
        l_ref[...] = jnp.zeros(l_ref.shape, jnp.float32)
        acc_ref[...] = jnp.zeros(acc_ref.shape, jnp.float32)
    else:
        m_ref[...] = m_in[...]
        l_ref[...] = l_in[...]
        acc_ref[...] = acc_in[...]

    def process(start, masked, visible=None):
        q = q_ref[...]
        k = kv_ref[pl.ds(start, tile), pl.ds(0, HEAD_SIZE)]
        v = kv_ref[pl.ds(start, tile), pl.ds(HEAD_SIZE, HEAD_SIZE)]
        s = lax.dot_general(k, q, (((1,), (1,)), ((), ())), preferred_element_type=jnp.float32)
        if masked:
            keys = lax.broadcasted_iota(jnp.int32, s.shape, 0) + start
            rows = lax.broadcasted_iota(jnp.int32, s.shape, 1)
            s = jnp.where(keys <= rows, s, jnp.float32(-1e30))
        if visible is not None:
            s = jnp.where(visible, s, -jnp.inf)
        m_old = m_ref[...]
        m_new = jnp.maximum(m_old, jnp.max(s, axis=0, keepdims=True))
        p = jnp.exp2((s - m_new) * exp_scale)
        factor = jnp.exp2((m_old - m_new) * exp_scale)
        l_ref[...] = l_ref[...] * factor + jnp.sum(p, axis=0, keepdims=True)
        pv = lax.dot_general(
            v, p.astype(jnp.bfloat16), (((0,), (0,)), ((), ())), preferred_element_type=jnp.float32
        )
        acc_ref[...] = acc_ref[...] * factor + pv
        m_ref[...] = m_new

    if back == 0:
        for t in range(block_len // tile):
            process(t * tile, True)
    else:
        for t in range(block_len // tile):
            process(t * tile, False, cycle_pos >= back)

    if last:
        o_refs[0][...] = (acc_ref[...] / l_ref[...]).T.astype(o_refs[0].dtype)
    else:
        o_refs[0][...] = m_ref[...]
        o_refs[1][...] = l_ref[...]
        o_refs[2][...] = acc_ref[...]


def attend(pos, qkv, kv, carry, q_heads, back, kv_col):
    block_len = qkv.shape[0]
    first = carry is None
    last = back == WINDOW_BLOCKS
    kernel = functools.partial(attend_kernel, block_len=block_len, back=back, first=first, last=last)
    row_spec = pl.BlockSpec((None, 1, block_len), lambda h, pos: (h, 0, 0))
    acc_spec = pl.BlockSpec((None, HEAD_SIZE, block_len), lambda h, pos: (h, 0, 0))
    in_specs = [
        pl.BlockSpec((block_len, HEAD_SIZE), lambda h, pos: (0, h)),
        pl.BlockSpec((block_len, 2 * HEAD_SIZE), lambda h, pos: (0, kv_col)),
    ]
    operands = [pos, qkv, kv]
    if not first:
        in_specs += [row_spec, row_spec, acc_spec]
        operands += list(carry)
    carry_shapes = [
        jax.ShapeDtypeStruct((q_heads, 1, block_len), jnp.float32),
        jax.ShapeDtypeStruct((q_heads, 1, block_len), jnp.float32),
        jax.ShapeDtypeStruct((q_heads, HEAD_SIZE, block_len), jnp.float32),
    ]
    if last:
        out_specs = [pl.BlockSpec((block_len, HEAD_SIZE), lambda h, pos: (0, h))]
        out_shape = [jax.ShapeDtypeStruct((block_len, q_heads * HEAD_SIZE), jnp.bfloat16)]
        aliases = {}
    else:
        out_specs = [row_spec, row_spec, acc_spec]
        out_shape = carry_shapes
        aliases = {} if first else {3: 0, 4: 1, 5: 2}
    grid_spec = pltpu.PrefetchScalarGridSpec(
        num_scalar_prefetch=1,
        grid=(q_heads,),
        in_specs=in_specs,
        out_specs=out_specs,
        scratch_shapes=[
            pltpu.VMEM((1, block_len), jnp.float32),
            pltpu.VMEM((1, block_len), jnp.float32),
            pltpu.VMEM((HEAD_SIZE, block_len), jnp.float32),
        ],
    )
    result = pl.pallas_call(
        kernel,
        grid_spec=grid_spec,
        out_shape=out_shape,
        input_output_aliases=aliases,
        compiler_params=pltpu.CompilerParams(dimension_semantics=("arbitrary",)),
    )(*operands)
    return result[0] if last else tuple(result)


def on_device(queries, keys, values):
    n = lax.axis_size("uly")
    rows = queries.shape[0]
    cycle_pos = lax.axis_index("ctx")
    packed = jnp.concatenate(
        [queries.reshape(rows, n, -1), keys.reshape(rows, n, -1), values.reshape(rows, n, -1)], axis=2
    )
    qkv = lax.all_to_all(packed, "uly", split_axis=1, concat_axis=0, tiled=True)
    qkv = qkv.reshape(rows * n, -1)
    q_heads = (qkv.shape[1] - 2 * HEAD_SIZE) // HEAD_SIZE
    pos = jnp.reshape(cycle_pos, (1,)).astype(jnp.int32)
    kv = qkv[:, q_heads * HEAD_SIZE:]
    carry = attend(pos, qkv, qkv, None, q_heads, 0, q_heads // 2)
    for back in range(1, WINDOW_BLOCKS + 1):
        kv = passed_along(kv, "ctx", 1)
        carry = attend(pos, qkv, kv, carry, q_heads, back, 0)
    return lax.all_to_all(carry, "uly", split_axis=0, concat_axis=1, tiled=True)


def solution(mesh):
    placed = (P(("ctx", "uly"), None), P(("ctx", "uly"), None), P(("ctx", "uly"), None))
    return jax.shard_map(
        on_device, mesh=mesh, in_specs=placed, out_specs=P(("ctx", "uly"), None), check_vma=False
    )
```

```python
import functools

import jax
import jax.numpy as jnp
from jax import lax
from jax.experimental import pallas as pl
from jax.experimental.pallas import tpu as pltpu
from jax.sharding import PartitionSpec as P


HEAD_SIZE = 128
WINDOW_BLOCKS = 3
KEY_TILE = 1024
LOG2_E = 1.4426950408889634


def passed_along(block, axis, distance):
    devices = range(lax.axis_size(axis))
    route = [(i - distance, i) for i in devices if i - distance in devices]
    return lax.ppermute(block, axis, route)


def attend_kernel(pos_ref, q_ref, kv_ref, *refs, block_len, back, last):
    if last:
        parts = [refs[3 * i:3 * i + 3] for i in range(WINDOW_BLOCKS)]
        o_ref = refs[3 * WINDOW_BLOCKS]
        m_ref, l_ref, acc_ref = refs[3 * WINDOW_BLOCKS + 1:]
    else:
        m_ref, l_ref, acc_ref = refs
    cycle_pos = pos_ref[0]
    exp_scale = HEAD_SIZE ** (-0.5) * LOG2_E
    tile = min(KEY_TILE, block_len)

    def process(start, masked, fresh):
        q = q_ref[...]
        k = kv_ref[pl.ds(start, tile), pl.ds(0, HEAD_SIZE)]
        v = kv_ref[pl.ds(start, tile), pl.ds(HEAD_SIZE, HEAD_SIZE)]
        s = lax.dot_general(k, q, (((1,), (1,)), ((), ())), preferred_element_type=jnp.float32)
        if masked:
            keys = lax.broadcasted_iota(jnp.int32, s.shape, 0) + start
            rows = lax.broadcasted_iota(jnp.int32, s.shape, 1)
            s = jnp.where(keys <= rows, s, jnp.float32(-1e30))
        if fresh:
            m_new = jnp.max(s, axis=0, keepdims=True)
        else:
            m_old = m_ref[...]
            m_new = jnp.maximum(m_old, jnp.max(s, axis=0, keepdims=True))
        p = jnp.exp2((s - m_new) * exp_scale)
        pv = lax.dot_general(
            v, p.astype(jnp.bfloat16), (((0,), (0,)), ((), ())), preferred_element_type=jnp.float32
        )
        if fresh:
            l_ref[...] = jnp.sum(p, axis=0, keepdims=True)
            acc_ref[...] = pv
        else:
            factor = jnp.exp2((m_old - m_new) * exp_scale)
            l_ref[...] = l_ref[...] * factor + jnp.sum(p, axis=0, keepdims=True)
            acc_ref[...] = acc_ref[...] * factor + pv
        m_ref[...] = m_new

    starts = [t * tile for t in range(block_len // tile)]
    if back == 0:
        for j, start in enumerate(starts):
            process(start, True, j == 0)
    else:
        @pl.when(cycle_pos >= back)
        def _():
            for j, start in enumerate(starts):
                process(start, False, j == 0)

        @pl.when(cycle_pos < back)
        def _():
            m_ref[...] = jnp.full(m_ref.shape, -jnp.inf, jnp.float32)
            l_ref[...] = jnp.zeros(l_ref.shape, jnp.float32)
            acc_ref[...] = jnp.zeros(acc_ref.shape, jnp.float32)

    if last:
        states = [(r[0][...], r[1][...], r[2][...]) for r in parts] + [(m_ref[...], l_ref[...], acc_ref[...])]
        m_all = states[0][0]
        for m_b, _, _ in states[1:]:
            m_all = jnp.maximum(m_all, m_b)
        total = jnp.zeros_like(m_all)
        acc = jnp.zeros(acc_ref.shape, jnp.float32)
        for m_b, l_b, acc_b in states:
            factor = jnp.exp2((m_b - m_all) * exp_scale)
            total = total + l_b * factor
            acc = acc + acc_b * factor
        o_ref[...] = (acc / total).T.astype(o_ref.dtype)


def attend(pos, q_src, kv, kv_col, q_heads, back, parts=None):
    block_len = q_src.shape[0]
    last = parts is not None
    kernel = functools.partial(attend_kernel, block_len=block_len, back=back, last=last)
    row_spec = pl.BlockSpec((None, 1, block_len), lambda h, pos: (h, 0, 0))
    acc_spec = pl.BlockSpec((None, HEAD_SIZE, block_len), lambda h, pos: (h, 0, 0))
    in_specs = [
        pl.BlockSpec((block_len, HEAD_SIZE), lambda h, pos: (0, h)),
        pl.BlockSpec((block_len, 2 * HEAD_SIZE), lambda h, pos: (0, kv_col)),
    ]
    operands = [pos, q_src, kv]
    state_shapes = [
        jax.ShapeDtypeStruct((q_heads, 1, block_len), jnp.float32),
        jax.ShapeDtypeStruct((q_heads, 1, block_len), jnp.float32),
        jax.ShapeDtypeStruct((q_heads, HEAD_SIZE, block_len), jnp.float32),
    ]
    if last:
        for part in parts:
            in_specs += [row_spec, row_spec, acc_spec]
            operands += list(part)
        out_specs = pl.BlockSpec((block_len, HEAD_SIZE), lambda h, pos: (0, h))
        out_shape = jax.ShapeDtypeStruct((block_len, q_heads * HEAD_SIZE), jnp.bfloat16)
        scratch = [
            pltpu.VMEM((1, block_len), jnp.float32),
            pltpu.VMEM((1, block_len), jnp.float32),
            pltpu.VMEM((HEAD_SIZE, block_len), jnp.float32),
        ]
    else:
        out_specs = [row_spec, row_spec, acc_spec]
        out_shape = state_shapes
        scratch = []
    grid_spec = pltpu.PrefetchScalarGridSpec(
        num_scalar_prefetch=1,
        grid=(q_heads,),
        in_specs=in_specs,
        out_specs=out_specs,
        scratch_shapes=scratch,
    )
    return pl.pallas_call(
        kernel,
        grid_spec=grid_spec,
        out_shape=out_shape,
        compiler_params=pltpu.CompilerParams(dimension_semantics=("arbitrary",)),
    )(*operands)


def on_device(queries, keys, values):
    n = lax.axis_size("uly")
    rows = queries.shape[0]
    cycle_pos = lax.axis_index("ctx")
    packed = jnp.concatenate(
        [queries.reshape(rows, n, -1), keys.reshape(rows, n, -1), values.reshape(rows, n, -1)], axis=2
    )
    qkv = lax.all_to_all(packed, "uly", split_axis=1, concat_axis=0, tiled=True)
    qkv = qkv.reshape(rows * n, -1)
    q_heads = (qkv.shape[1] - 2 * HEAD_SIZE) // HEAD_SIZE
    pos = jnp.reshape(cycle_pos, (1,)).astype(jnp.int32)
    kv = qkv[:, q_heads * HEAD_SIZE:]
    parts = [attend(pos, qkv, qkv, q_heads // 2, q_heads, 0)]
    for back in range(1, WINDOW_BLOCKS + 1):
        kv = passed_along(kv, "ctx", 1)
        last = back == WINDOW_BLOCKS
        parts.append(attend(pos, qkv, kv, 0, q_heads, back, parts if last else None))
    return lax.all_to_all(parts[-1], "uly", split_axis=0, concat_axis=1, tiled=True)


def solution(mesh):
    placed = (P(("ctx", "uly"), None), P(("ctx", "uly"), None), P(("ctx", "uly"), None))
    return jax.shard_map(
        on_device, mesh=mesh, in_specs=placed, out_specs=P(("ctx", "uly"), None), check_vma=False
    )
```

```python
import functools

import jax
import jax.numpy as jnp
from jax import lax
from jax.experimental import pallas as pl
from jax.experimental.pallas import tpu as pltpu
from jax.sharding import PartitionSpec as P


HEAD_SIZE = 128
WINDOW_BLOCKS = 3
KEY_TILE = 1024
LOG2_E = 1.4426950408889634


def passed_along(block, axis, distance):
    devices = range(lax.axis_size(axis))
    route = [(i - distance, i) for i in devices if i - distance in devices]
    return lax.ppermute(block, axis, route)


def attend_kernel(pos_ref, q_ref, kv_ref, *refs, block_len, back, last):
    if last:
        parts = [refs[3 * i:3 * i + 3] for i in range(WINDOW_BLOCKS)]
        o_ref = refs[3 * WINDOW_BLOCKS]
        m_ref, l_ref, acc_ref = refs[3 * WINDOW_BLOCKS + 1:]
    else:
        m_ref, l_ref, acc_ref = refs
    cycle_pos = pos_ref[0]
    exp_scale = HEAD_SIZE ** (-0.5) * LOG2_E
    tile = min(KEY_TILE, block_len)

    def process(start, masked, fresh):
        q = q_ref[...]
        k = kv_ref[pl.ds(start, tile), pl.ds(0, HEAD_SIZE)]
        v = kv_ref[pl.ds(start, tile), pl.ds(HEAD_SIZE, HEAD_SIZE)]
        s = lax.dot_general(k, q, (((1,), (1,)), ((), ())), preferred_element_type=jnp.float32)
        if masked:
            keys = lax.broadcasted_iota(jnp.int32, s.shape, 0) + start
            rows = lax.broadcasted_iota(jnp.int32, s.shape, 1)
            s = jnp.where(keys <= rows, s, jnp.float32(-1e30))
        if fresh:
            m_new = jnp.max(s, axis=0, keepdims=True)
        else:
            m_old = m_ref[...]
            m_new = jnp.maximum(m_old, jnp.max(s, axis=0, keepdims=True))
        p = jnp.exp2((s - m_new) * exp_scale)
        pv = lax.dot_general(
            v, p.astype(jnp.bfloat16), (((0,), (0,)), ((), ())), preferred_element_type=jnp.float32
        )
        if fresh:
            l_ref[...] = jnp.sum(p, axis=0, keepdims=True)
            acc_ref[...] = pv
        else:
            factor = jnp.exp2((m_old - m_new) * exp_scale)
            l_ref[...] = l_ref[...] * factor + jnp.sum(p, axis=0, keepdims=True)
            acc_ref[...] = acc_ref[...] * factor + pv
        m_ref[...] = m_new

    starts = [t * tile for t in range(block_len // tile)]
    if back == 0:
        for j, start in enumerate(starts):
            process(start, True, j == 0)
    else:
        for j, start in enumerate(starts):
            process(start, False, j == 0)

    if last:
        states = [(r[0][...], r[1][...], r[2][...]) for r in parts] + [(m_ref[...], l_ref[...], acc_ref[...])]
        seen = [cycle_pos >= b for b in range(len(states))]
        m_all = states[0][0]
        for b in range(1, len(states)):
            m_all = jnp.maximum(m_all, jnp.where(seen[b], states[b][0], -jnp.inf))
        total = jnp.zeros_like(m_all)
        acc = jnp.zeros(acc_ref.shape, jnp.float32)
        for b, (m_b, l_b, acc_b) in enumerate(states):
            factor = jnp.exp2((m_b - m_all) * exp_scale)
            total = total + jnp.where(seen[b], l_b * factor, 0.0)
            acc = acc + jnp.where(seen[b], acc_b * factor, 0.0)
        o_ref[...] = (acc / total).T.astype(o_ref.dtype)


def attend(pos, q_src, kv, kv_col, q_heads, back, parts=None):
    block_len = q_src.shape[0]
    last = parts is not None
    kernel = functools.partial(attend_kernel, block_len=block_len, back=back, last=last)
    row_spec = pl.BlockSpec((None, 1, block_len), lambda h, pos: (h, 0, 0))
    acc_spec = pl.BlockSpec((None, HEAD_SIZE, block_len), lambda h, pos: (h, 0, 0))
    in_specs = [
        pl.BlockSpec((block_len, HEAD_SIZE), lambda h, pos: (0, h)),
        pl.BlockSpec((block_len, 2 * HEAD_SIZE), lambda h, pos: (0, kv_col)),
    ]
    operands = [pos, q_src, kv]
    state_shapes = [
        jax.ShapeDtypeStruct((q_heads, 1, block_len), jnp.float32),
        jax.ShapeDtypeStruct((q_heads, 1, block_len), jnp.float32),
        jax.ShapeDtypeStruct((q_heads, HEAD_SIZE, block_len), jnp.float32),
    ]
    if last:
        for part in parts:
            in_specs += [row_spec, row_spec, acc_spec]
            operands += list(part)
        out_specs = pl.BlockSpec((block_len, HEAD_SIZE), lambda h, pos: (0, h))
        out_shape = jax.ShapeDtypeStruct((block_len, q_heads * HEAD_SIZE), jnp.bfloat16)
        scratch = [
            pltpu.VMEM((1, block_len), jnp.float32),
            pltpu.VMEM((1, block_len), jnp.float32),
            pltpu.VMEM((HEAD_SIZE, block_len), jnp.float32),
        ]
    else:
        out_specs = [row_spec, row_spec, acc_spec]
        out_shape = state_shapes
        scratch = []
    grid_spec = pltpu.PrefetchScalarGridSpec(
        num_scalar_prefetch=1,
        grid=(q_heads,),
        in_specs=in_specs,
        out_specs=out_specs,
        scratch_shapes=scratch,
    )
    return pl.pallas_call(
        kernel,
        grid_spec=grid_spec,
        out_shape=out_shape,
        compiler_params=pltpu.CompilerParams(dimension_semantics=("arbitrary",)),
    )(*operands)


def on_device(queries, keys, values):
    n = lax.axis_size("uly")
    rows = queries.shape[0]
    cycle_pos = lax.axis_index("ctx")
    packed = jnp.concatenate(
        [queries.reshape(rows, n, -1), keys.reshape(rows, n, -1), values.reshape(rows, n, -1)], axis=2
    )
    qkv = lax.all_to_all(packed, "uly", split_axis=1, concat_axis=0, tiled=True)
    qkv = qkv.reshape(rows * n, -1)
    q_heads = (qkv.shape[1] - 2 * HEAD_SIZE) // HEAD_SIZE
    pos = jnp.reshape(cycle_pos, (1,)).astype(jnp.int32)
    kv_own = qkv[:, q_heads * HEAD_SIZE:]
    parts = [attend(pos, qkv, qkv, q_heads // 2, q_heads, 0)]
    for back in range(1, WINDOW_BLOCKS + 1):
        kv = passed_along(kv_own, "ctx", back)
        last = back == WINDOW_BLOCKS
        parts.append(attend(pos, qkv, kv, 0, q_heads, back, parts if last else None))
    return lax.all_to_all(parts[-1], "uly", split_axis=0, concat_axis=1, tiled=True)


def solution(mesh):
    placed = (P(("ctx", "uly"), None), P(("ctx", "uly"), None), P(("ctx", "uly"), None))
    return jax.shard_map(
        on_device, mesh=mesh, in_specs=placed, out_specs=P(("ctx", "uly"), None), check_vma=False
    )
```

```python
import functools

import jax
import jax.numpy as jnp
from jax import lax
from jax.experimental import pallas as pl
from jax.experimental.pallas import tpu as pltpu
from jax.sharding import PartitionSpec as P


HEAD_SIZE = 128
WINDOW_BLOCKS = 3
KEY_TILE = 1024
LOG2_E = 1.4426950408889634


def passed_along(block, axis, distance):
    devices = range(lax.axis_size(axis))
    route = [(i - distance, i) for i in devices if i - distance in devices]
    return lax.ppermute(block, axis, route)


def attend_kernel(pos_ref, q_ref, kv_ref, *refs, block_len, back, last):
    if last:
        parts = [refs[3 * i:3 * i + 3] for i in range(WINDOW_BLOCKS)]
        o_ref = refs[3 * WINDOW_BLOCKS]
        m_ref, l_ref, acc_ref = refs[3 * WINDOW_BLOCKS + 1:]
    else:
        m_ref, l_ref, acc_ref = refs
    cycle_pos = pos_ref[0]
    exp_scale = HEAD_SIZE ** (-0.5) * LOG2_E
    tile = min(KEY_TILE, block_len)

    def process(start, masked, fresh):
        q = q_ref[...]
        k = kv_ref[pl.ds(start, tile), pl.ds(0, HEAD_SIZE)]
        v = kv_ref[pl.ds(start, tile), pl.ds(HEAD_SIZE, HEAD_SIZE)]
        s = lax.dot_general(k, q, (((1,), (1,)), ((), ())), preferred_element_type=jnp.float32)
        if masked:
            keys = lax.broadcasted_iota(jnp.int32, s.shape, 0) + start
            rows = lax.broadcasted_iota(jnp.int32, s.shape, 1)
            s = jnp.where(keys <= rows, s, jnp.float32(-1e30))
        if fresh:
            m_new = jnp.max(s, axis=0, keepdims=True)
        else:
            m_old = m_ref[...]
            m_new = jnp.maximum(m_old, jnp.max(s, axis=0, keepdims=True))
        p = jnp.exp2(s * exp_scale - m_new * exp_scale)
        pv = lax.dot_general(
            v, p.astype(jnp.bfloat16), (((0,), (0,)), ((), ())), preferred_element_type=jnp.float32
        )
        if fresh:
            l_ref[...] = jnp.sum(p, axis=0, keepdims=True)
            acc_ref[...] = pv
        else:
            factor = jnp.exp2((m_old - m_new) * exp_scale)
            l_ref[...] = l_ref[...] * factor + jnp.sum(p, axis=0, keepdims=True)
            acc_ref[...] = acc_ref[...] * factor + pv
        m_ref[...] = m_new

    starts = [t * tile for t in range(block_len // tile)]
    if back == 0:
        for j, start in enumerate(starts):
            process(start, True, j == 0)
    else:
        for j, start in enumerate(starts):
            process(start, False, j == 0)

    if last:
        states = [(r[0][...], r[1][...], r[2][...]) for r in parts] + [(m_ref[...], l_ref[...], acc_ref[...])]
        seen = [cycle_pos >= b for b in range(len(states))]
        m_all = states[0][0]
        for b in range(1, len(states)):
            m_all = jnp.maximum(m_all, jnp.where(seen[b], states[b][0], -jnp.inf))
        total = jnp.zeros_like(m_all)
        acc = jnp.zeros(acc_ref.shape, jnp.float32)
        for b, (m_b, l_b, acc_b) in enumerate(states):
            factor = jnp.exp2((m_b - m_all) * exp_scale)
            total = total + jnp.where(seen[b], l_b * factor, 0.0)
            acc = acc + jnp.where(seen[b], acc_b * factor, 0.0)
        o_ref[...] = (acc / total).T.astype(o_ref.dtype)


def attend(pos, q_src, kv, kv_col, q_heads, back, parts=None):
    block_len = q_src.shape[0]
    last = parts is not None
    kernel = functools.partial(attend_kernel, block_len=block_len, back=back, last=last)
    row_spec = pl.BlockSpec((None, 1, block_len), lambda h, pos: (h, 0, 0))
    acc_spec = pl.BlockSpec((None, HEAD_SIZE, block_len), lambda h, pos: (h, 0, 0))
    in_specs = [
        pl.BlockSpec((block_len, HEAD_SIZE), lambda h, pos: (0, h)),
        pl.BlockSpec((block_len, 2 * HEAD_SIZE), lambda h, pos: (0, kv_col)),
    ]
    operands = [pos, q_src, kv]
    state_shapes = [
        jax.ShapeDtypeStruct((q_heads, 1, block_len), jnp.float32),
        jax.ShapeDtypeStruct((q_heads, 1, block_len), jnp.float32),
        jax.ShapeDtypeStruct((q_heads, HEAD_SIZE, block_len), jnp.float32),
    ]
    if last:
        for part in parts:
            in_specs += [row_spec, row_spec, acc_spec]
            operands += list(part)
        out_specs = pl.BlockSpec((block_len, HEAD_SIZE), lambda h, pos: (0, h))
        out_shape = jax.ShapeDtypeStruct((block_len, q_heads * HEAD_SIZE), jnp.bfloat16)
        scratch = [
            pltpu.VMEM((1, block_len), jnp.float32),
            pltpu.VMEM((1, block_len), jnp.float32),
            pltpu.VMEM((HEAD_SIZE, block_len), jnp.float32),
        ]
    else:
        out_specs = [row_spec, row_spec, acc_spec]
        out_shape = state_shapes
        scratch = []
    grid_spec = pltpu.PrefetchScalarGridSpec(
        num_scalar_prefetch=1,
        grid=(q_heads,),
        in_specs=in_specs,
        out_specs=out_specs,
        scratch_shapes=scratch,
    )
    return pl.pallas_call(
        kernel,
        grid_spec=grid_spec,
        out_shape=out_shape,
        compiler_params=pltpu.CompilerParams(dimension_semantics=("arbitrary",)),
    )(*operands)


def on_device(queries, keys, values):
    n = lax.axis_size("uly")
    rows = queries.shape[0]
    cycle_pos = lax.axis_index("ctx")
    packed = jnp.concatenate(
        [queries.reshape(rows, n, -1), keys.reshape(rows, n, -1), values.reshape(rows, n, -1)], axis=2
    )
    qkv = lax.all_to_all(packed, "uly", split_axis=1, concat_axis=0, tiled=True)
    qkv = qkv.reshape(rows * n, -1)
    q_heads = (qkv.shape[1] - 2 * HEAD_SIZE) // HEAD_SIZE
    pos = jnp.reshape(cycle_pos, (1,)).astype(jnp.int32)
    kv = qkv[:, q_heads * HEAD_SIZE:]
    parts = [attend(pos, qkv, qkv, q_heads // 2, q_heads, 0)]
    for back in range(1, WINDOW_BLOCKS + 1):
        kv = passed_along(kv, "ctx", 1)
        last = back == WINDOW_BLOCKS
        parts.append(attend(pos, qkv, kv, 0, q_heads, back, parts if last else None))
    return lax.all_to_all(parts[-1], "uly", split_axis=0, concat_axis=1, tiled=True)


def solution(mesh):
    placed = (P(("ctx", "uly"), None), P(("ctx", "uly"), None), P(("ctx", "uly"), None))
    return jax.shard_map(
        on_device, mesh=mesh, in_specs=placed, out_specs=P(("ctx", "uly"), None), check_vma=False
    )
```

```python
import functools

import jax
import jax.numpy as jnp
from jax import lax
from jax.experimental import pallas as pl
from jax.experimental.pallas import tpu as pltpu
from jax.sharding import PartitionSpec as P


HEAD_SIZE = 128
WINDOW_BLOCKS = 3
KEY_TILE = 1024
LOG2_E = 1.4426950408889634


def passed_along(block, axis, distance):
    devices = range(lax.axis_size(axis))
    route = [(i - distance, i) for i in devices if i - distance in devices]
    return lax.ppermute(block, axis, route)


def attend_kernel(pos_ref, q_ref, kv_ref, *refs, block_len, back, last):
    if last:
        parts = [refs[3 * i:3 * i + 3] for i in range(WINDOW_BLOCKS)]
        o_ref = refs[3 * WINDOW_BLOCKS]
        m_ref, l_ref, acc_ref = refs[3 * WINDOW_BLOCKS + 1:]
    else:
        m_ref, l_ref, acc_ref = refs
    cycle_pos = pos_ref[0]
    exp_scale = HEAD_SIZE ** (-0.5) * LOG2_E
    tile = min(KEY_TILE, block_len)

    def process(start, masked, fresh):
        q = q_ref[...]
        k = kv_ref[pl.ds(start, tile), pl.ds(0, HEAD_SIZE)]
        v = kv_ref[pl.ds(start, tile), pl.ds(HEAD_SIZE, HEAD_SIZE)]
        s = lax.dot_general(k, q, (((1,), (1,)), ((), ())), preferred_element_type=jnp.float32)
        if masked:
            keys = lax.broadcasted_iota(jnp.int32, s.shape, 0) + start
            rows = lax.broadcasted_iota(jnp.int32, s.shape, 1)
            s = jnp.where(keys <= rows, s, jnp.float32(-1e30))
        if fresh:
            m_new = jnp.max(s, axis=0, keepdims=True)
        else:
            m_old = m_ref[...]
            m_new = jnp.maximum(m_old, jnp.max(s, axis=0, keepdims=True))
        p = jnp.exp2((s - m_new) * exp_scale)
        pv = lax.dot_general(
            v, p.astype(jnp.bfloat16), (((0,), (0,)), ((), ())), preferred_element_type=jnp.float32
        )
        if fresh:
            l_ref[...] = jnp.sum(p, axis=0, keepdims=True)
            acc_ref[...] = pv
        else:
            factor = jnp.exp2((m_old - m_new) * exp_scale)
            l_ref[...] = l_ref[...] * factor + jnp.sum(p, axis=0, keepdims=True)
            acc_ref[...] = acc_ref[...] * factor + pv
        m_ref[...] = m_new

    def process_diag(start, width, q_lo, fresh):
        q = q_ref[pl.ds(q_lo, block_len - q_lo), :]
        k = kv_ref[pl.ds(start, width), pl.ds(0, HEAD_SIZE)]
        v = kv_ref[pl.ds(start, width), pl.ds(HEAD_SIZE, HEAD_SIZE)]
        s = lax.dot_general(k, q, (((1,), (1,)), ((), ())), preferred_element_type=jnp.float32)
        keys = lax.broadcasted_iota(jnp.int32, s.shape, 0) + start
        rows = lax.broadcasted_iota(jnp.int32, s.shape, 1) + q_lo
        s = jnp.where(keys <= rows, s, jnp.float32(-1e30))
        cols = pl.ds(q_lo, block_len - q_lo)
        if fresh:
            m_new = jnp.max(s, axis=0, keepdims=True)
        else:
            m_old = m_ref[:, cols]
            m_new = jnp.maximum(m_old, jnp.max(s, axis=0, keepdims=True))
        p = jnp.exp2((s - m_new) * exp_scale)
        pv = lax.dot_general(
            v, p.astype(jnp.bfloat16), (((0,), (0,)), ((), ())), preferred_element_type=jnp.float32
        )
        if fresh:
            l_ref[...] = jnp.sum(p, axis=0, keepdims=True)
            acc_ref[...] = pv
        else:
            factor = jnp.exp2((m_old - m_new) * exp_scale)
            l_ref[:, cols] = l_ref[:, cols] * factor + jnp.sum(p, axis=0, keepdims=True)
            acc_ref[:, cols] = acc_ref[:, cols] * factor + pv
        m_ref[:, cols] = m_new

    starts = [t * tile for t in range(block_len // tile)]
    if back == 0:
        half = block_len // 2
        process_diag(0, half, 0, True)
        process_diag(half, half, half, False)
    else:
        for j, start in enumerate(starts):
            process(start, False, j == 0)

    if last:
        states = [(r[0][...], r[1][...], r[2][...]) for r in parts] + [(m_ref[...], l_ref[...], acc_ref[...])]
        seen = [cycle_pos >= b for b in range(len(states))]
        m_all = states[0][0]
        for b in range(1, len(states)):
            m_all = jnp.maximum(m_all, jnp.where(seen[b], states[b][0], -jnp.inf))
        total = jnp.zeros_like(m_all)
        acc = jnp.zeros(acc_ref.shape, jnp.float32)
        for b, (m_b, l_b, acc_b) in enumerate(states):
            factor = jnp.exp2((m_b - m_all) * exp_scale)
            total = total + jnp.where(seen[b], l_b * factor, 0.0)
            acc = acc + jnp.where(seen[b], acc_b * factor, 0.0)
        o_ref[...] = (acc / total).T.astype(o_ref.dtype)


def attend(pos, q_src, kv, kv_col, q_heads, back, parts=None):
    block_len = q_src.shape[0]
    last = parts is not None
    kernel = functools.partial(attend_kernel, block_len=block_len, back=back, last=last)
    row_spec = pl.BlockSpec((None, 1, block_len), lambda h, pos: (h, 0, 0))
    acc_spec = pl.BlockSpec((None, HEAD_SIZE, block_len), lambda h, pos: (h, 0, 0))
    in_specs = [
        pl.BlockSpec((block_len, HEAD_SIZE), lambda h, pos: (0, h)),
        pl.BlockSpec((block_len, 2 * HEAD_SIZE), lambda h, pos: (0, kv_col)),
    ]
    operands = [pos, q_src, kv]
    state_shapes = [
        jax.ShapeDtypeStruct((q_heads, 1, block_len), jnp.float32),
        jax.ShapeDtypeStruct((q_heads, 1, block_len), jnp.float32),
        jax.ShapeDtypeStruct((q_heads, HEAD_SIZE, block_len), jnp.float32),
    ]
    if last:
        for part in parts:
            in_specs += [row_spec, row_spec, acc_spec]
            operands += list(part)
        out_specs = pl.BlockSpec((block_len, HEAD_SIZE), lambda h, pos: (0, h))
        out_shape = jax.ShapeDtypeStruct((block_len, q_heads * HEAD_SIZE), jnp.bfloat16)
        scratch = [
            pltpu.VMEM((1, block_len), jnp.float32),
            pltpu.VMEM((1, block_len), jnp.float32),
            pltpu.VMEM((HEAD_SIZE, block_len), jnp.float32),
        ]
    else:
        out_specs = [row_spec, row_spec, acc_spec]
        out_shape = state_shapes
        scratch = []
    grid_spec = pltpu.PrefetchScalarGridSpec(
        num_scalar_prefetch=1,
        grid=(q_heads,),
        in_specs=in_specs,
        out_specs=out_specs,
        scratch_shapes=scratch,
    )
    return pl.pallas_call(
        kernel,
        grid_spec=grid_spec,
        out_shape=out_shape,
        compiler_params=pltpu.CompilerParams(dimension_semantics=("arbitrary",)),
    )(*operands)


def on_device(queries, keys, values):
    n = lax.axis_size("uly")
    rows = queries.shape[0]
    cycle_pos = lax.axis_index("ctx")
    packed = jnp.concatenate(
        [queries.reshape(rows, n, -1), keys.reshape(rows, n, -1), values.reshape(rows, n, -1)], axis=2
    )
    qkv = lax.all_to_all(packed, "uly", split_axis=1, concat_axis=0, tiled=True)
    qkv = qkv.reshape(rows * n, -1)
    q_heads = (qkv.shape[1] - 2 * HEAD_SIZE) // HEAD_SIZE
    pos = jnp.reshape(cycle_pos, (1,)).astype(jnp.int32)
    kv = qkv[:, q_heads * HEAD_SIZE:]
    parts = [attend(pos, qkv, qkv, q_heads // 2, q_heads, 0)]
    for back in range(1, WINDOW_BLOCKS + 1):
        kv = passed_along(kv, "ctx", 1)
        last = back == WINDOW_BLOCKS
        parts.append(attend(pos, qkv, kv, 0, q_heads, back, parts if last else None))
    return lax.all_to_all(parts[-1], "uly", split_axis=0, concat_axis=1, tiled=True)


def solution(mesh):
    placed = (P(("ctx", "uly"), None), P(("ctx", "uly"), None), P(("ctx", "uly"), None))
    return jax.shard_map(
        on_device, mesh=mesh, in_specs=placed, out_specs=P(("ctx", "uly"), None), check_vma=False
    )
```

```python
import functools

import jax
import jax.numpy as jnp
from jax import lax
from jax.experimental import pallas as pl
from jax.experimental.pallas import tpu as pltpu
from jax.sharding import PartitionSpec as P


HEAD_SIZE = 128
WINDOW_BLOCKS = 3
KEY_TILE = 1024
LOG2_E = 1.4426950408889634
HEADS_PER_STEP = 2


def passed_along(block, axis, distance):
    devices = range(lax.axis_size(axis))
    route = [(i - distance, i) for i in devices if i - distance in devices]
    return lax.ppermute(block, axis, route)


def attend_kernel(pos_ref, q_ref, kv_ref, *refs, block_len, back, last, hps=1):
    if last:
        parts = [refs[3 * i:3 * i + 3] for i in range(WINDOW_BLOCKS)]
        o_ref = refs[3 * WINDOW_BLOCKS]
        m_ref, l_ref, acc_ref = refs[3 * WINDOW_BLOCKS + 1:]
    else:
        m_ref, l_ref, acc_ref = refs
    cycle_pos = pos_ref[0]
    exp_scale = HEAD_SIZE ** (-0.5) * LOG2_E
    tile = min(KEY_TILE, block_len)

    def process(start, masked, fresh, hh=0):
        q = q_ref[:, pl.ds(hh * HEAD_SIZE, HEAD_SIZE)]
        mr, lr, ar = (m_ref.at[hh], l_ref.at[hh], acc_ref.at[hh]) if not last else (m_ref, l_ref, acc_ref)
        return _process(q, mr, lr, ar, start, masked, fresh)

    def _process(q, m_ref, l_ref, acc_ref, start, masked, fresh):
        k = kv_ref[pl.ds(start, tile), pl.ds(0, HEAD_SIZE)]
        v = kv_ref[pl.ds(start, tile), pl.ds(HEAD_SIZE, HEAD_SIZE)]
        s = lax.dot_general(k, q, (((1,), (1,)), ((), ())), preferred_element_type=jnp.float32)
        if masked:
            keys = lax.broadcasted_iota(jnp.int32, s.shape, 0) + start
            rows = lax.broadcasted_iota(jnp.int32, s.shape, 1)
            s = jnp.where(keys <= rows, s, jnp.float32(-1e30))
        if fresh:
            m_new = jnp.max(s, axis=0, keepdims=True)
        else:
            m_old = m_ref[...]
            m_new = jnp.maximum(m_old, jnp.max(s, axis=0, keepdims=True))
        p = jnp.exp2((s - m_new) * exp_scale)
        pv = lax.dot_general(
            v, p.astype(jnp.bfloat16), (((0,), (0,)), ((), ())), preferred_element_type=jnp.float32
        )
        if fresh:
            l_ref[...] = jnp.sum(p, axis=0, keepdims=True)
            acc_ref[...] = pv
        else:
            factor = jnp.exp2((m_old - m_new) * exp_scale)
            l_ref[...] = l_ref[...] * factor + jnp.sum(p, axis=0, keepdims=True)
            acc_ref[...] = acc_ref[...] * factor + pv
        m_ref[...] = m_new

    starts = [t * tile for t in range(block_len // tile)]
    for hh in range(hps):
        for j, start in enumerate(starts):
            process(start, back == 0, j == 0, hh)

    if last:
        states = [(r[0][...], r[1][...], r[2][...]) for r in parts] + [(m_ref[...], l_ref[...], acc_ref[...])]
        seen = [cycle_pos >= b for b in range(len(states))]
        m_all = states[0][0]
        for b in range(1, len(states)):
            m_all = jnp.maximum(m_all, jnp.where(seen[b], states[b][0], -jnp.inf))
        total = jnp.zeros_like(m_all)
        acc = jnp.zeros(acc_ref.shape, jnp.float32)
        for b, (m_b, l_b, acc_b) in enumerate(states):
            factor = jnp.exp2((m_b - m_all) * exp_scale)
            total = total + jnp.where(seen[b], l_b * factor, 0.0)
            acc = acc + jnp.where(seen[b], acc_b * factor, 0.0)
        o_ref[...] = (acc / total).T.astype(o_ref.dtype)


def attend(pos, q_src, kv, kv_col, q_heads, back, parts=None):
    block_len = q_src.shape[0]
    last = parts is not None
    hps = 1 if last else HEADS_PER_STEP
    kernel = functools.partial(attend_kernel, block_len=block_len, back=back, last=last, hps=hps)
    row_spec = pl.BlockSpec((None, 1, block_len), lambda h, pos: (h, 0, 0))
    acc_spec = pl.BlockSpec((None, HEAD_SIZE, block_len), lambda h, pos: (h, 0, 0))
    if not last:
        row_spec = pl.BlockSpec((hps, 1, block_len), lambda h, pos: (h, 0, 0))
        acc_spec = pl.BlockSpec((hps, HEAD_SIZE, block_len), lambda h, pos: (h, 0, 0))
    in_specs = [
        pl.BlockSpec((block_len, hps * HEAD_SIZE), lambda h, pos: (0, h)),
        pl.BlockSpec((block_len, 2 * HEAD_SIZE), lambda h, pos: (0, kv_col)),
    ]
    operands = [pos, q_src, kv]
    state_shapes = [
        jax.ShapeDtypeStruct((q_heads, 1, block_len), jnp.float32),
        jax.ShapeDtypeStruct((q_heads, 1, block_len), jnp.float32),
        jax.ShapeDtypeStruct((q_heads, HEAD_SIZE, block_len), jnp.float32),
    ]
    if last:
        for part in parts:
            in_specs += [row_spec, row_spec, acc_spec]
            operands += list(part)
        out_specs = pl.BlockSpec((block_len, HEAD_SIZE), lambda h, pos: (0, h))
        out_shape = jax.ShapeDtypeStruct((block_len, q_heads * HEAD_SIZE), jnp.bfloat16)
        scratch = [
            pltpu.VMEM((1, block_len), jnp.float32),
            pltpu.VMEM((1, block_len), jnp.float32),
            pltpu.VMEM((HEAD_SIZE, block_len), jnp.float32),
        ]
    else:
        out_specs = [row_spec, row_spec, acc_spec]
        out_shape = state_shapes
        scratch = []
    grid_spec = pltpu.PrefetchScalarGridSpec(
        num_scalar_prefetch=1,
        grid=(q_heads // hps,),
        in_specs=in_specs,
        out_specs=out_specs,
        scratch_shapes=scratch,
    )
    return pl.pallas_call(
        kernel,
        grid_spec=grid_spec,
        out_shape=out_shape,
        compiler_params=pltpu.CompilerParams(dimension_semantics=("arbitrary",)),
    )(*operands)


def on_device(queries, keys, values):
    n = lax.axis_size("uly")
    rows = queries.shape[0]
    cycle_pos = lax.axis_index("ctx")
    packed = jnp.concatenate(
        [queries.reshape(rows, n, -1), keys.reshape(rows, n, -1), values.reshape(rows, n, -1)], axis=2
    )
    qkv = lax.all_to_all(packed, "uly", split_axis=1, concat_axis=0, tiled=True)
    qkv = qkv.reshape(rows * n, -1)
    q_heads = (qkv.shape[1] - 2 * HEAD_SIZE) // HEAD_SIZE
    pos = jnp.reshape(cycle_pos, (1,)).astype(jnp.int32)
    kv = qkv[:, q_heads * HEAD_SIZE:]
    parts = [attend(pos, qkv, qkv, q_heads // 2, q_heads, 0)]
    for back in range(1, WINDOW_BLOCKS + 1):
        kv = jnp.concatenate(
            [passed_along(kv[:, :HEAD_SIZE], "ctx", 1), passed_along(kv[:, HEAD_SIZE:], "ctx", 1)], axis=1
        )
        last = back == WINDOW_BLOCKS
        parts.append(attend(pos, qkv, kv, 0, q_heads, back, parts if last else None))
    return lax.all_to_all(parts[-1], "uly", split_axis=0, concat_axis=1, tiled=True)


def solution(mesh):
    placed = (P(("ctx", "uly"), None), P(("ctx", "uly"), None), P(("ctx", "uly"), None))
    return jax.shard_map(
        on_device, mesh=mesh, in_specs=placed, out_specs=P(("ctx", "uly"), None), check_vma=False
    )
```

```python
import functools

import jax
import jax.numpy as jnp
from jax import lax
from jax.experimental import pallas as pl
from jax.experimental.pallas import tpu as pltpu
from jax.sharding import PartitionSpec as P


HEAD_SIZE = 128
WINDOW_BLOCKS = 3
KEY_TILE = 1024
LOG2_E = 1.4426950408889634
HEADS_PER_STEP = 2


def passed_along(block, axis, distance):
    devices = range(lax.axis_size(axis))
    route = [(i - distance, i) for i in devices if i - distance in devices]
    return lax.ppermute(block, axis, route)


def attend_kernel(pos_ref, q_ref, kv_ref, *refs, block_len, back, last, hps=1):
    if last:
        parts = [refs[3 * i:3 * i + 3] for i in range(WINDOW_BLOCKS)]
        o_ref = refs[3 * WINDOW_BLOCKS]
        m_ref, l_ref, acc_ref = refs[3 * WINDOW_BLOCKS + 1:]
    else:
        m_ref, l_ref, acc_ref = refs
    cycle_pos = pos_ref[0]
    exp_scale = HEAD_SIZE ** (-0.5) * LOG2_E
    tile = min(KEY_TILE, block_len)

    def process(start, masked, fresh, hh=0):
        q = q_ref[:, pl.ds(hh * HEAD_SIZE, HEAD_SIZE)]
        mr, lr, ar = m_ref.at[hh], l_ref.at[hh], acc_ref.at[hh]
        return _process(q, mr, lr, ar, start, masked, fresh)

    def _process(q, m_ref, l_ref, acc_ref, start, masked, fresh):
        k = kv_ref[pl.ds(start, tile), pl.ds(0, HEAD_SIZE)]
        v = kv_ref[pl.ds(start, tile), pl.ds(HEAD_SIZE, HEAD_SIZE)]
        s = lax.dot_general(k, q, (((1,), (1,)), ((), ())), preferred_element_type=jnp.float32)
        if masked:
            keys = lax.broadcasted_iota(jnp.int32, s.shape, 0) + start
            rows = lax.broadcasted_iota(jnp.int32, s.shape, 1)
            s = jnp.where(keys <= rows, s, jnp.float32(-1e30))
        if fresh:
            m_new = jnp.max(s, axis=0, keepdims=True)
        else:
            m_old = m_ref[...]
            m_new = jnp.maximum(m_old, jnp.max(s, axis=0, keepdims=True))
        p = jnp.exp2((s - m_new) * exp_scale)
        pv = lax.dot_general(
            v, p.astype(jnp.bfloat16), (((0,), (0,)), ((), ())), preferred_element_type=jnp.float32
        )
        if fresh:
            l_ref[...] = jnp.sum(p, axis=0, keepdims=True)
            acc_ref[...] = pv
        else:
            factor = jnp.exp2((m_old - m_new) * exp_scale)
            l_ref[...] = l_ref[...] * factor + jnp.sum(p, axis=0, keepdims=True)
            acc_ref[...] = acc_ref[...] * factor + pv
        m_ref[...] = m_new

    starts = [t * tile for t in range(block_len // tile)]
    for hh in range(hps):
        for j, start in enumerate(starts):
            process(start, back == 0, j == 0, hh)

    if last:
        seen = [cycle_pos >= b for b in range(WINDOW_BLOCKS + 1)]
        for hh in range(hps):
            states = [(r[0][hh], r[1][hh], r[2][hh]) for r in parts] + [(m_ref[hh], l_ref[hh], acc_ref[hh])]
            m_all = states[0][0]
            for b in range(1, len(states)):
                m_all = jnp.maximum(m_all, jnp.where(seen[b], states[b][0], -jnp.inf))
            total = jnp.zeros_like(m_all)
            acc = jnp.zeros(acc_ref.shape[1:], jnp.float32)
            for b, (m_b, l_b, acc_b) in enumerate(states):
                factor = jnp.exp2((m_b - m_all) * exp_scale)
                total = total + jnp.where(seen[b], l_b * factor, 0.0)
                acc = acc + jnp.where(seen[b], acc_b * factor, 0.0)
            o_ref[:, pl.ds(hh * HEAD_SIZE, HEAD_SIZE)] = (acc / total).T.astype(o_ref.dtype)


def attend(pos, q_src, kv, kv_col, q_heads, back, parts=None):
    block_len = q_src.shape[0]
    last = parts is not None
    hps = HEADS_PER_STEP
    kernel = functools.partial(attend_kernel, block_len=block_len, back=back, last=last, hps=hps)
    row_spec = pl.BlockSpec((hps, 1, block_len), lambda h, pos: (h, 0, 0))
    acc_spec = pl.BlockSpec((hps, HEAD_SIZE, block_len), lambda h, pos: (h, 0, 0))
    in_specs = [
        pl.BlockSpec((block_len, hps * HEAD_SIZE), lambda h, pos: (0, h)),
        pl.BlockSpec((block_len, 2 * HEAD_SIZE), lambda h, pos: (0, kv_col)),
    ]
    operands = [pos, q_src, kv]
    state_shapes = [
        jax.ShapeDtypeStruct((q_heads, 1, block_len), jnp.float32),
        jax.ShapeDtypeStruct((q_heads, 1, block_len), jnp.float32),
        jax.ShapeDtypeStruct((q_heads, HEAD_SIZE, block_len), jnp.float32),
    ]
    if last:
        for part in parts:
            in_specs += [row_spec, row_spec, acc_spec]
            operands += list(part)
        out_specs = pl.BlockSpec((block_len, hps * HEAD_SIZE), lambda h, pos: (0, h))
        out_shape = jax.ShapeDtypeStruct((block_len, q_heads * HEAD_SIZE), jnp.bfloat16)
        scratch = [
            pltpu.VMEM((hps, 1, block_len), jnp.float32),
            pltpu.VMEM((hps, 1, block_len), jnp.float32),
            pltpu.VMEM((hps, HEAD_SIZE, block_len), jnp.float32),
        ]
    else:
        out_specs = [row_spec, row_spec, acc_spec]
        out_shape = state_shapes
        scratch = []
    grid_spec = pltpu.PrefetchScalarGridSpec(
        num_scalar_prefetch=1,
        grid=(q_heads // hps,),
        in_specs=in_specs,
        out_specs=out_specs,
        scratch_shapes=scratch,
    )
    return pl.pallas_call(
        kernel,
        grid_spec=grid_spec,
        out_shape=out_shape,
        compiler_params=pltpu.CompilerParams(dimension_semantics=("arbitrary",)),
    )(*operands)


def on_device(queries, keys, values):
    n = lax.axis_size("uly")
    rows = queries.shape[0]
    cycle_pos = lax.axis_index("ctx")
    packed = jnp.concatenate(
        [queries.reshape(rows, n, -1), keys.reshape(rows, n, -1), values.reshape(rows, n, -1)], axis=2
    )
    qkv = lax.all_to_all(packed, "uly", split_axis=1, concat_axis=0, tiled=True)
    qkv = qkv.reshape(rows * n, -1)
    q_heads = (qkv.shape[1] - 2 * HEAD_SIZE) // HEAD_SIZE
    pos = jnp.reshape(cycle_pos, (1,)).astype(jnp.int32)
    kv = qkv[:, q_heads * HEAD_SIZE:]
    parts = [attend(pos, qkv, qkv, q_heads // 2, q_heads, 0)]
    for back in range(1, WINDOW_BLOCKS + 1):
        kv = passed_along(kv, "ctx", 1)
        last = back == WINDOW_BLOCKS
        parts.append(attend(pos, qkv, kv, 0, q_heads, back, parts if last else None))
    return lax.all_to_all(parts[-1], "uly", split_axis=0, concat_axis=1, tiled=True)


def solution(mesh):
    placed = (P(("ctx", "uly"), None), P(("ctx", "uly"), None), P(("ctx", "uly"), None))
    return jax.shard_map(
        on_device, mesh=mesh, in_specs=placed, out_specs=P(("ctx", "uly"), None), check_vma=False
    )
```
